512 devices in a mesh: row: 32 (over x, z), col: 16 (over y, core).
Axes of the slice: x: 4, y: 8, z: 8, core: 2. Of those that a mesh axis runs over, the one named last changes fastest.
Arguments:
- matrix: float32 [14336, 14336], P('row', 'col'), may hold values from -3 to 3
- reflectors: float32 [1, 64, 14336], P(None, None, 'row'), may hold values from -0.09375 to 0.09375
- factors: float32 [1, 64, 64], replicated, may hold values from -0.1 to 2, as said below
Outputs:
- updated: float32 [14336, 14336], P('row', 'col')
- companions: float32 [1, 64, 14336], P(None, None, 'row')
The draws below stay inside these ranges and needn't reach their ends.
Inputs may be any that keep to these rules, and one draw needn't show every extreme that they name: `factors`: each factor is upper triangular (zero below the diagonal) with diagonal entries between 1 and 2.
All inputs are finite; a program needn't handle non-finite values.
Results may differ from the reference program's by a relative error of at most 0.0001.
Values sent between devices are 32-bit elements; how exact they have to be, the bound alone decides.
No kernel may reach another device: no remote copies, remote signals or barrier semaphores. Data moves between devices by JAX's collectives and lax.ppermute only.
A program may use at most 64 MiB of HBM per device.

```python
import math
import jax
import jax.numpy as jnp
from jax import lax

B = 64
PANELS = 1
N = 14336


def draw_matrix(key, part):
    first_key = jax.random.fold_in(jax.random.fold_in(key, 11), 0)
    base = jnp.clip(jax.random.normal(first_key, (N, N), jnp.float32), -4.0, 4.0)
    return 0.5 * (base + base.T) / math.sqrt(2.0)


def draw_factors(key, part):
    first_key, second_key = jax.random.split(jax.random.fold_in(key, 23))
    diagonal = jax.random.uniform(first_key, (PANELS, B), jnp.float32, 1.0, 2.0)
    upper = jax.random.uniform(second_key, (PANELS, B, B), jnp.float32, -0.1, 0.1)
    strict = jnp.triu(jnp.ones((B, B), jnp.float32), 1)
    return upper * strict[None, :, :] + diagonal[:, :, None] * jnp.eye(B, dtype=jnp.float32)[None, :, :]


def steps_of(rng, dims, pieces, least, top_value):
    def one(dim, parts):
        steps = jax.random.uniform(jax.random.fold_in(jax.random.fold_in(rng, 6), dim), (parts,), jnp.float32, least / len(pieces), top_value / len(pieces))
        return jnp.repeat(jnp.exp(steps), dims[dim] // parts).reshape((-1,) + (1,) * (len(dims) - dim - 1))

    gain = one(*pieces[0])
    for cut in pieces[1:]:
        gain = gain * one(*cut)
    return gain


def bell_draw(stream_key, shape, scale, most, cuts=(), kind=jnp.bfloat16):
    values = scale * jax.random.normal(stream_key, shape, jnp.float32)
    if cuts:
        values = values * steps_of(stream_key, shape, cuts, -0.22, 0.18)
    return jnp.clip(values, -most, most).astype(kind)


def setup_inputs(seed: int = 0) -> dict:
    streams_of = jax.random.split(jax.random.key(seed), 4)
    matrix = draw_matrix(jax.random.fold_in(streams_of[3], 71), 0)
    reflectors = bell_draw(streams_of[1], (PANELS, B, N), (N // 4) ** -0.5, 0.09375, ((2, 32),), jnp.float32)
    factors = draw_factors(jax.random.fold_in(streams_of[3], 71), 0)
    return {"matrix": matrix, "reflectors": reflectors, "factors": factors}


def contract(left_side, right_side, left_dim, right_dim):
    return lax.dot_general(left_side, right_side, (((left_dim,), (right_dim,)), ((), ())), precision=lax.Precision.HIGHEST, preferred_element_type=jnp.float32)


def reference(matrix, reflectors, factors):
    current = matrix
    results = []
    for step_index in range(PANELS):
        v_rows = reflectors[step_index]
        factor = factors[step_index]
        y_rows = contract(v_rows, current, 1, 1)
        x_rows = contract(factor, y_rows, 0, 0)
        projected = contract(v_rows, x_rows, 1, 1)
        mixing = contract(projected, factor, 0, 0)
        w_rows = x_rows - 0.5 * contract(mixing, v_rows, 1, 0)
        current = current - contract(v_rows, w_rows, 0, 0) - contract(w_rows, v_rows, 0, 0)
        results.append(w_rows)
    return current, jnp.stack(results)
```

```python
import jax
import jax.numpy as jnp
from jax import lax
from jax.sharding import PartitionSpec as P


def contract(left_side, right_side, left_dim, right_dim):
    return lax.dot_general(
        left_side,
        right_side,
        (((left_dim,), (right_dim,)), ((), ())),
        precision=lax.Precision.HIGHEST,
        preferred_element_type=jnp.float32,
    )


def column_block_pairs(rows, cols, shift):
    group = rows // cols
    pairs = []
    for r in range(rows):
        for c in range(cols):
            target_row = group * c + (r % group - shift) % group
            pairs.append((r * cols + c, target_row * cols + r // group))
    return pairs


def to_column_blocks(values, rows, cols):
    group = rows // cols
    rounds = [
        lax.ppermute(values, ("row", "col"), column_block_pairs(rows, cols, shift))
        for shift in range(group)
    ]
    offset = lax.axis_index("row") % group
    blocks = []
    for part in range(group):
        block = rounds[0]
        for shift in range(1, group):
            block = jnp.where((part - offset) % group == shift, rounds[shift], block)
        blocks.append(block)
    return jnp.concatenate(blocks, axis=values.ndim - 1)


def make_shards(rows, cols):
    def shards(matrix, reflectors, factors):
        current = matrix
        v_rows = reflectors[0]
        factor = factors[0]
        v_cols = to_column_blocks(v_rows, rows, cols)
        partial_value = contract(v_cols, current, 1, 1)
        row_sums = jnp.sum(lax.all_gather(partial_value, "col"), axis=0)
        x_rows = contract(factor, row_sums, 0, 0)
        x_cols = to_column_blocks(x_rows, rows, cols)
        projected = jnp.sum(lax.all_gather(contract(v_rows, x_rows, 1, 1), "row"), axis=0)
        mixing = contract(projected, factor, 0, 0)
        w_rows = x_rows - 0.5 * contract(mixing, v_rows, 1, 0)
        w_cols = x_cols - 0.5 * contract(mixing, v_cols, 1, 0)
        current = current - contract(v_rows, w_cols, 0, 0) - contract(w_rows, v_cols, 0, 0)
        return (current, jnp.stack([w_rows]))

    return shards


def solution(mesh):
    return jax.shard_map(
        make_shards(mesh.shape["row"], mesh.shape["col"]),
        mesh=mesh,
        in_specs=(P("row", "col"), P(None, None, "row"), P()),
        out_specs=(P("row", "col"), P(None, None, "row")),
        check_vma=False,
    )
```

```python
import jax
import jax.numpy as jnp
from jax import lax
from jax.sharding import Mesh
from jax.sharding import PartitionSpec as P


def contract(left_side, right_side, left_dim, right_dim):
    return lax.dot_general(
        left_side,
        right_side,
        (((left_dim,), (right_dim,)), ((), ())),
        precision=lax.Precision.HIGHEST,
        preferred_element_type=jnp.float32,
    )


def gathered_sum(values, axes):
    for axis in axes:
        values = jnp.sum(lax.all_gather(values, axis), axis=0)
    return values


def column_block_pairs(rows, cols, shift):
    group = rows // cols
    pairs = []
    for r in range(rows):
        for c in range(cols):
            target_row = group * c + (r % group - shift) % group
            pairs.append((r * cols + c, target_row * cols + r // group))
    return pairs


def to_column_blocks(values, rows, cols, all_axes, row_index):
    group = rows // cols
    rounds = [
        lax.ppermute(values, all_axes, column_block_pairs(rows, cols, shift))
        for shift in range(group)
    ]
    offset = row_index % group
    blocks = []
    for part in range(group):
        block = rounds[0]
        for shift in range(1, group):
            block = jnp.where((part - offset) % group == shift, rounds[shift], block)
        blocks.append(block)
    return jnp.concatenate(blocks, axis=values.ndim - 1)


def make_shards(row_axes, col_axes, rows, cols):
    all_axes = tuple(row_axes) + tuple(col_axes)

    def shards(matrix, reflectors, factors):
        current = matrix
        v_rows = reflectors[0]
        factor = factors[0]
        row_index = lax.axis_index(tuple(row_axes))
        v_cols = to_column_blocks(v_rows, rows, cols, all_axes, row_index)
        col_sums = gathered_sum(contract(v_rows, current, 1, 0), row_axes[::-1])
        partial_value = contract(v_cols, current, 1, 1)
        partial_inner = contract(v_cols, col_sums, 1, 1)
        width = partial_value.shape[1]
        sums = gathered_sum(jnp.concatenate([partial_value, partial_inner], axis=1), col_axes[::-1])
        row_sums = sums[:, :width]
        inner = sums[:, width:]
        x_rows = contract(factor, row_sums, 0, 0)
        x_cols = contract(factor, col_sums, 0, 0)
        projected = contract(inner, factor, 0, 0)
        mixing = contract(projected, factor, 0, 0)
        w_rows = x_rows - 0.5 * contract(mixing, v_rows, 1, 0)
        w_cols = x_cols - 0.5 * contract(mixing, v_cols, 1, 0)
        current = current - contract(v_rows, w_cols, 0, 0) - contract(w_rows, v_cols, 0, 0)
        return (current, jnp.stack([w_rows]))

    return shards


def solution(mesh):
    row_axes, col_axes = ("x", "z"), ("y", "core")
    rows, cols = mesh.shape["row"], mesh.shape["col"]
    split = (4, rows // 4, cols // 2, 2) if rows % 4 == 0 and cols % 2 == 0 else None
    if split is None:
        row_axes, col_axes = ("row",), ("col",)
        fine = mesh
    else:
        fine = Mesh(mesh.devices.reshape(split), row_axes + col_axes)
    return jax.shard_map(
        make_shards(row_axes, col_axes, rows, cols),
        mesh=fine,
        in_specs=(P(row_axes, col_axes), P(None, None, row_axes), P()),
        out_specs=(P(row_axes, col_axes), P(None, None, row_axes)),
        check_vma=False,
    )
```

```python
import jax
import jax.numpy as jnp
from jax import lax
from jax.sharding import Mesh
from jax.sharding import PartitionSpec as P


def contract(left_side, right_side, left_dim, right_dim):
    return lax.dot_general(
        left_side,
        right_side,
        (((left_dim,), (right_dim,)), ((), ())),
        precision=lax.Precision.HIGHEST,
        preferred_element_type=jnp.float32,
    )


def gathered_sum(values, axes):
    for axis in axes:
        values = jnp.sum(lax.all_gather(values, axis), axis=0)
    return values


def split_sum(values, axis, split_axis):
    width = values.shape[1] // 2
    mine = jnp.where(lax.axis_index(split_axis) == 0, values[:, :width], values[:, width:])
    total = gathered_sum(mine, (axis,))
    both = lax.all_gather(total, split_axis)
    return jnp.concatenate([both[0], both[1]], axis=1)


def scattered_sum(values, axis, parts):
    chunks = values.reshape((parts, values.shape[0] // parts) + values.shape[1:])
    mine = jnp.sum(lax.all_to_all(chunks, axis, 0, 0, tiled=False), axis=0)
    return lax.all_gather(mine, axis, tiled=True)


def halves_sum(values, axis):
    width = values.shape[1] // 2
    left = gathered_sum(values[:, :width], (axis,))
    right = gathered_sum(values[:, width:], (axis,))
    return jnp.concatenate([left, right], axis=1)


def column_block_pairs(rows, cols, shift):
    group = rows // cols
    pairs = []
    for r in range(rows):
        for c in range(cols):
            target_row = group * c + (r % group - shift) % group
            pairs.append((r * cols + c, target_row * cols + r // group))
    return pairs


def to_column_blocks(values, rows, cols, all_axes, row_index):
    group = rows // cols
    rounds = [
        lax.ppermute(values, all_axes, column_block_pairs(rows, cols, shift))
        for shift in range(group)
    ]
    offset = row_index % group
    blocks = []
    for part in range(group):
        block = rounds[0]
        for shift in range(1, group):
            block = jnp.where((part - offset) % group == shift, rounds[shift], block)
        blocks.append(block)
    return jnp.concatenate(blocks, axis=values.ndim - 1)


def make_shards(row_axes, col_axes, rows, cols):
    all_axes = tuple(row_axes) + tuple(col_axes)

    def shards(matrix, reflectors, factors):
        current = matrix
        v_rows = reflectors[0]
        factor = factors[0]
        row_index = lax.axis_index(tuple(row_axes))
        v_cols = to_column_blocks(v_rows, rows, cols, all_axes, row_index)
        col_sums = scattered_sum(gathered_sum(contract(v_rows, current, 1, 0), row_axes[:1]), row_axes[1], lax.axis_size(row_axes[1]))
        partial_value = contract(v_cols, current, 1, 1)
        partial_inner = contract(v_cols, col_sums, 1, 1)
        width = partial_value.shape[1]
        sums = split_sum(gathered_sum(jnp.concatenate([partial_value, partial_inner], axis=1), col_axes[1:]), col_axes[0], col_axes[1])
        row_sums = sums[:, :width]
        inner = sums[:, width:]
        x_rows = contract(factor, row_sums, 0, 0)
        x_cols = contract(factor, col_sums, 0, 0)
        projected = contract(inner, factor, 0, 0)
        mixing = contract(projected, factor, 0, 0)
        w_rows = x_rows - 0.5 * contract(mixing, v_rows, 1, 0)
        w_cols = x_cols - 0.5 * contract(mixing, v_cols, 1, 0)
        current = current - contract(v_rows, w_cols, 0, 0) - contract(w_rows, v_cols, 0, 0)
        return (current, jnp.stack([w_rows]))

    return shards


def solution(mesh):
    row_axes, col_axes = ("x", "z"), ("y", "core")
    rows, cols = mesh.shape["row"], mesh.shape["col"]
    split = (4, rows // 4, cols // 2, 2) if rows % 4 == 0 and cols % 2 == 0 else None
    if split is None:
        row_axes, col_axes = ("row",), ("col",)
        fine = mesh
    else:
        fine = Mesh(mesh.devices.reshape(split), row_axes + col_axes)
    return jax.shard_map(
        make_shards(row_axes, col_axes, rows, cols),
        mesh=fine,
        in_specs=(P(row_axes, col_axes), P(None, None, row_axes), P()),
        out_specs=(P(row_axes, col_axes), P(None, None, row_axes)),
        check_vma=False,
    )
```

```python
import jax
import jax.numpy as jnp
from jax import lax
from jax.sharding import Mesh
from jax.sharding import PartitionSpec as P


def contract(left_side, right_side, left_dim, right_dim):
    return lax.dot_general(
        left_side,
        right_side,
        (((left_dim,), (right_dim,)), ((), ())),
        precision=lax.Precision.HIGHEST,
        preferred_element_type=jnp.float32,
    )


def gathered_sum(values, axes):
    for axis in axes:
        values = jnp.sum(lax.all_gather(values, axis), axis=0)
    return values


def split_sum(values, axis, split_axis):
    width = values.shape[1] // 2
    mine = jnp.where(lax.axis_index(split_axis) == 0, values[:, :width], values[:, width:])
    total = gathered_sum(mine, (axis,))
    both = lax.all_gather(total, split_axis)
    return jnp.concatenate([both[0], both[1]], axis=1)


def scattered_sum(values, axis, parts):
    chunks = values.reshape((parts, values.shape[0] // parts) + values.shape[1:])
    mine = jnp.sum(lax.all_to_all(chunks, axis, 0, 0, tiled=False), axis=0)
    return lax.all_gather(mine, axis, tiled=True)


def halves_sum(values, axis):
    width = values.shape[1] // 2
    left = gathered_sum(values[:, :width], (axis,))
    right = gathered_sum(values[:, width:], (axis,))
    return jnp.concatenate([left, right], axis=1)


def column_block_pairs(rows, cols, shift):
    group = rows // cols
    pairs = []
    for r in range(rows):
        for c in range(cols):
            target_row = group * c + (r % group - shift) % group
            pairs.append((r * cols + c, target_row * cols + r // group))
    return pairs


def staged_route(rows, cols):
    sizes = (4, rows // 4, cols // 2, 2)
    if rows % 4 or cols % 2 or sizes[2] % sizes[0]:
        return None
    k = sizes[2] // sizes[0]

    def split(i):
        return (i // (sizes[1] * sizes[2] * 2), (i // (sizes[2] * 2)) % sizes[1], (i // 2) % sizes[2], i % 2)

    def join(x, z, y, core):
        return ((x * sizes[1] + z) * sizes[2] + y) * 2 + core

    def hop(i):
        x, z, y, core = split(i)
        return join(y // k, z, k * x + y % k, core)

    return [(i, hop(i)) for i in range(rows * cols)]


def to_column_blocks(values, rows, cols, all_axes, row_index):
    group = rows // cols
    first = staged_route(rows, cols)
    if first is None:
        rounds = [
            lax.ppermute(values, all_axes, column_block_pairs(rows, cols, shift))
            for shift in range(group)
        ]
    else:
        moved = lax.ppermute(values, all_axes, first)
        rounds = []
        for shift in range(group):
            final = dict(column_block_pairs(rows, cols, shift))
            rounds.append(lax.ppermute(moved, all_axes, [(mid, final[i]) for i, mid in first]))
    offset = row_index % group
    blocks = []
    for part in range(group):
        block = rounds[0]
        for shift in range(1, group):
            block = jnp.where((part - offset) % group == shift, rounds[shift], block)
        blocks.append(block)
    return jnp.concatenate(blocks, axis=values.ndim - 1)


def make_shards(row_axes, col_axes, rows, cols):
    all_axes = tuple(row_axes) + tuple(col_axes)

    def shards(matrix, reflectors, factors):
        current = matrix
        v_rows = reflectors[0]
        factor = factors[0]
        row_index = lax.axis_index(tuple(row_axes))
        v_cols = to_column_blocks(v_rows, rows, cols, all_axes, row_index)
        col_sums = scattered_sum(gathered_sum(contract(v_rows, current, 1, 0), row_axes[:1]), row_axes[1], lax.axis_size(row_axes[1]))
        partial_value = contract(v_cols, current, 1, 1)
        partial_inner = contract(v_cols, col_sums, 1, 1)
        width = partial_value.shape[1]
        sums = split_sum(gathered_sum(jnp.concatenate([partial_value, partial_inner], axis=1), col_axes[1:]), col_axes[0], col_axes[1])
        row_sums = sums[:, :width]
        inner = sums[:, width:]
        x_rows = contract(factor, row_sums, 0, 0)
        x_cols = contract(factor, col_sums, 0, 0)
        projected = contract(inner, factor, 0, 0)
        mixing = contract(projected, factor, 0, 0)
        w_rows = x_rows - 0.5 * contract(mixing, v_rows, 1, 0)
        w_cols = x_cols - 0.5 * contract(mixing, v_cols, 1, 0)
        current = current - contract(v_rows, w_cols, 0, 0) - contract(w_rows, v_cols, 0, 0)
        return (current, jnp.stack([w_rows]))

    return shards


def solution(mesh):
    row_axes, col_axes = ("x", "z"), ("y", "core")
    rows, cols = mesh.shape["row"], mesh.shape["col"]
    split = (4, rows // 4, cols // 2, 2) if rows % 4 == 0 and cols % 2 == 0 else None
    if split is None:
        row_axes, col_axes = ("row",), ("col",)
        fine = mesh
    else:
        fine = Mesh(mesh.devices.reshape(split), row_axes + col_axes)
    return jax.shard_map(
        make_shards(row_axes, col_axes, rows, cols),
        mesh=fine,
        in_specs=(P(row_axes, col_axes), P(None, None, row_axes), P()),
        out_specs=(P(row_axes, col_axes), P(None, None, row_axes)),
        check_vma=False,
    )
```

```python
import jax
import jax.numpy as jnp
from jax import lax
from jax.sharding import Mesh
from jax.sharding import PartitionSpec as P


def contract(left_side, right_side, left_dim, right_dim):
    return lax.dot_general(
        left_side,
        right_side,
        (((left_dim,), (right_dim,)), ((), ())),
        precision=lax.Precision.HIGHEST,
        preferred_element_type=jnp.float32,
    )


def gathered_sum(values, axes):
    for axis in axes:
        values = jnp.sum(lax.all_gather(values, axis), axis=0)
    return values


def split_sum(values, axis, split_axis):
    width = values.shape[1] // 2
    mine = jnp.where(lax.axis_index(split_axis) == 0, values[:, :width], values[:, width:])
    total = gathered_sum(mine, (axis,))
    both = lax.all_gather(total, split_axis)
    return jnp.concatenate([both[0], both[1]], axis=1)


def scattered_sum(values, axis, parts):
    chunks = values.reshape((parts, values.shape[0] // parts) + values.shape[1:])
    mine = jnp.sum(lax.all_to_all(chunks, axis, 0, 0, tiled=False), axis=0)
    return lax.all_gather(mine, axis, tiled=True)


def scattered_sum_nested(values, axes):
    if not axes:
        return values
    parts = lax.axis_size(axes[0])
    chunks = values.reshape((parts, values.shape[0] // parts) + values.shape[1:])
    mine = jnp.sum(lax.all_to_all(chunks, axes[0], 0, 0, tiled=False), axis=0)
    mine = scattered_sum_nested(mine, axes[1:])
    return lax.all_gather(mine, axes[0], tiled=True)


def halves_sum(values, axis):
    width = values.shape[1] // 2
    left = gathered_sum(values[:, :width], (axis,))
    right = gathered_sum(values[:, width:], (axis,))
    return jnp.concatenate([left, right], axis=1)


def column_block_pairs(rows, cols, shift):
    group = rows // cols
    pairs = []
    for r in range(rows):
        for c in range(cols):
            target_row = group * c + (r % group - shift) % group
            pairs.append((r * cols + c, target_row * cols + r // group))
    return pairs


def staged_route(rows, cols):
    sizes = (4, rows // 4, cols // 2, 2)
    if rows % 4 or cols % 2 or sizes[2] % sizes[0]:
        return None
    k = sizes[2] // sizes[0]

    def split(i):
        return (i // (sizes[1] * sizes[2] * 2), (i // (sizes[2] * 2)) % sizes[1], (i // 2) % sizes[2], i % 2)

    def join(x, z, y, core):
        return ((x * sizes[1] + z) * sizes[2] + y) * 2 + core

    def hop(i):
        x, z, y, core = split(i)
        return join(y // k, z, k * x + y % k, core)

    return [(i, hop(i)) for i in range(rows * cols)]


def to_column_blocks(values, rows, cols, all_axes, row_index):
    group = rows // cols
    first = staged_route(rows, cols)
    if first is None:
        rounds = [
            lax.ppermute(values, all_axes, column_block_pairs(rows, cols, shift))
            for shift in range(group)
        ]
    else:
        moved = lax.ppermute(values, all_axes, first)
        rounds = []
        for shift in range(group):
            final = dict(column_block_pairs(rows, cols, shift))
            rounds.append(lax.ppermute(moved, all_axes, [(mid, final[i]) for i, mid in first]))
    offset = row_index % group
    blocks = []
    for part in range(group):
        block = rounds[0]
        for shift in range(1, group):
            block = jnp.where((part - offset) % group == shift, rounds[shift], block)
        blocks.append(block)
    return jnp.concatenate(blocks, axis=values.ndim - 1)


def make_shards(row_axes, col_axes, rows, cols):
    all_axes = tuple(row_axes) + tuple(col_axes)

    def shards(matrix, reflectors, factors):
        current = matrix
        v_rows = reflectors[0]
        factor = factors[0]
        row_index = lax.axis_index(tuple(row_axes))
        v_cols = to_column_blocks(v_rows, rows, cols, all_axes, row_index)
        col_sums = scattered_sum_nested(gathered_sum(contract(v_rows, current, 1, 0), row_axes[:1]), row_axes[:0:-1])
        partial_value = contract(v_cols, current, 1, 1)
        partial_inner = contract(v_cols, col_sums, 1, 1)
        width = partial_value.shape[1]
        sums = split_sum(gathered_sum(jnp.concatenate([partial_value, partial_inner], axis=1), col_axes[1:]), col_axes[0], col_axes[1])
        row_sums = sums[:, :width]
        inner = sums[:, width:]
        x_rows = contract(factor, row_sums, 0, 0)
        x_cols = contract(factor, col_sums, 0, 0)
        projected = contract(inner, factor, 0, 0)
        mixing = contract(projected, factor, 0, 0)
        w_rows = x_rows - 0.5 * contract(mixing, v_rows, 1, 0)
        w_cols = x_cols - 0.5 * contract(mixing, v_cols, 1, 0)
        current = current - contract(v_rows, w_cols, 0, 0) - contract(w_rows, v_cols, 0, 0)
        return (current, jnp.stack([w_rows]))

    return shards


def solution(mesh):
    rows, cols = mesh.shape["row"], mesh.shape["col"]
    row_axes, col_axes = ("x", "za", "zb"), ("y", "core")
    fine = Mesh(mesh.devices.reshape((4, rows // 8, 2, cols // 2, 2)), row_axes + col_axes)
    return jax.shard_map(
        make_shards(row_axes, col_axes, rows, cols),
        mesh=fine,
        in_specs=(P(row_axes, col_axes), P(None, None, row_axes), P()),
        out_specs=(P(row_axes, col_axes), P(None, None, row_axes)),
        check_vma=False,
    )
```

```python
import jax
import jax.numpy as jnp
from jax import lax
from jax.sharding import Mesh
from jax.sharding import PartitionSpec as P


def contract(left_side, right_side, left_dim, right_dim, precision=lax.Precision.HIGHEST):
    return lax.dot_general(
        left_side,
        right_side,
        (((left_dim,), (right_dim,)), ((), ())),
        precision=precision,
        preferred_element_type=jnp.float32,
    )


def contract_matrix(left_side, right_side, left_dim, right_dim):
    return contract(left_side, right_side, left_dim, right_dim, lax.Precision.HIGH)


def gathered_sum(values, axes):
    for axis in axes:
        values = jnp.sum(lax.all_gather(values, axis), axis=0)
    return values


def split_sum(values, axis, split_axis):
    width = values.shape[1] // 2
    mine = jnp.where(lax.axis_index(split_axis) == 0, values[:, :width], values[:, width:])
    total = gathered_sum(mine, (axis,))
    both = lax.all_gather(total, split_axis)
    return jnp.concatenate([both[0], both[1]], axis=1)


def scattered_sum(values, axis, parts):
    chunks = values.reshape((parts, values.shape[0] // parts) + values.shape[1:])
    mine = jnp.sum(lax.all_to_all(chunks, axis, 0, 0, tiled=False), axis=0)
    return lax.all_gather(mine, axis, tiled=True)


def scattered_sum_nested(values, axes, inner_axes=()):
    if not axes:
        return gathered_sum(values, inner_axes)
    parts = lax.axis_size(axes[0])
    chunks = values.reshape((parts, values.shape[0] // parts) + values.shape[1:])
    mine = jnp.sum(lax.all_to_all(chunks, axes[0], 0, 0, tiled=False), axis=0)
    mine = scattered_sum_nested(mine, axes[1:], inner_axes)
    return lax.all_gather(mine, axes[0], tiled=True)


def halves_sum(values, axis):
    width = values.shape[1] // 2
    left = gathered_sum(values[:, :width], (axis,))
    right = gathered_sum(values[:, width:], (axis,))
    return jnp.concatenate([left, right], axis=1)


def column_block_pairs(rows, cols, shift):
    group = rows // cols
    pairs = []
    for r in range(rows):
        for c in range(cols):
            target_row = group * c + (r % group - shift) % group
            pairs.append((r * cols + c, target_row * cols + r // group))
    return pairs


def staged_route(rows, cols):
    sizes = (4, rows // 4, cols // 2, 2)
    if rows % 4 or cols % 2 or sizes[2] % sizes[0]:
        return None
    k = sizes[2] // sizes[0]

    def split(i):
        return (i // (sizes[1] * sizes[2] * 2), (i // (sizes[2] * 2)) % sizes[1], (i // 2) % sizes[2], i % 2)

    def join(x, z, y, core):
        return ((x * sizes[1] + z) * sizes[2] + y) * 2 + core

    def hop(i):
        x, z, y, core = split(i)
        return join(y // k, z, k * x + y % k, core)

    return [(i, hop(i)) for i in range(rows * cols)]


def to_column_blocks(values, rows, cols, all_axes, row_index):
    group = rows // cols
    first = staged_route(rows, cols)
    if first is None:
        rounds = [
            lax.ppermute(values, all_axes, column_block_pairs(rows, cols, shift))
            for shift in range(group)
        ]
    else:
        moved = lax.ppermute(values, all_axes, first)
        rounds = []
        for shift in range(group):
            final = dict(column_block_pairs(rows, cols, shift))
            rounds.append(lax.ppermute(moved, all_axes, [(mid, final[i]) for i, mid in first]))
    offset = row_index % group
    blocks = []
    for part in range(group):
        block = rounds[0]
        for shift in range(1, group):
            block = jnp.where((part - offset) % group == shift, rounds[shift], block)
        blocks.append(block)
    return jnp.concatenate(blocks, axis=values.ndim - 1)


def make_shards(row_axes, col_axes, rows, cols):
    all_axes = tuple(row_axes) + tuple(col_axes)

    def shards(matrix, reflectors, factors):
        current = matrix
        v_rows = reflectors[0]
        factor = factors[0]
        row_index = lax.axis_index(tuple(row_axes))
        v_cols = to_column_blocks(v_rows, rows, cols, all_axes, row_index)
        col_sums = scattered_sum_nested(contract_matrix(v_rows, current, 1, 0), row_axes[:0:-1], row_axes[:1])
        partial_value = contract_matrix(v_cols, current, 1, 1)
        partial_inner = contract(v_cols, col_sums, 1, 1)
        width = partial_value.shape[1]
        sums = split_sum(gathered_sum(jnp.concatenate([partial_value, partial_inner], axis=1), col_axes[1:]), col_axes[0], col_axes[1])
        row_sums = sums[:, :width]
        inner = sums[:, width:]
        x_rows = contract(factor, row_sums, 0, 0)
        x_cols = contract(factor, col_sums, 0, 0)
        projected = contract(inner, factor, 0, 0)
        mixing = contract(projected, factor, 0, 0)
        w_rows = x_rows - 0.5 * contract(mixing, v_rows, 1, 0)
        w_cols = x_cols - 0.5 * contract(mixing, v_cols, 1, 0)
        current = current - contract_matrix(v_rows, w_cols, 0, 0) - contract_matrix(w_rows, v_cols, 0, 0)
        return (current, jnp.stack([w_rows]))

    return shards


def solution(mesh):
    rows, cols = mesh.shape["row"], mesh.shape["col"]
    row_axes, col_axes = ("x", "za", "zb"), ("y", "core")
    fine = Mesh(mesh.devices.reshape((4, rows // 8, 2, cols // 2, 2)), row_axes + col_axes)
    return jax.shard_map(
        make_shards(row_axes, col_axes, rows, cols),
        mesh=fine,
        in_specs=(P(row_axes, col_axes), P(None, None, row_axes), P()),
        out_specs=(P(row_axes, col_axes), P(None, None, row_axes)),
        check_vma=False,
    )
```

```python
import jax
import jax.numpy as jnp
from jax import lax
from jax.sharding import Mesh
from jax.sharding import PartitionSpec as P


def contract(left_side, right_side, left_dim, right_dim):
    return lax.dot_general(
        left_side,
        right_side,
        (((left_dim,), (right_dim,)), ((), ())),
        precision=lax.Precision.HIGHEST,
        preferred_element_type=jnp.float32,
    )


def gathered_sum(values, axes):
    for axis in axes:
        values = jnp.sum(lax.all_gather(values, axis), axis=0)
    return values


def split_sum(values, axis, split_axis):
    width = values.shape[1] // 2
    mine = jnp.where(lax.axis_index(split_axis) == 0, values[:, :width], values[:, width:])
    total = gathered_sum(mine, (axis,))
    both = lax.all_gather(total, split_axis)
    return jnp.concatenate([both[0], both[1]], axis=1)


def scattered_sum(values, axis, parts):
    chunks = values.reshape((parts, values.shape[0] // parts) + values.shape[1:])
    mine = jnp.sum(lax.all_to_all(chunks, axis, 0, 0, tiled=False), axis=0)
    return lax.all_gather(mine, axis, tiled=True)


def scattered_sum_nested(values, axes, inner_axes=()):
    if not axes:
        return gathered_sum(values, inner_axes)
    parts = lax.axis_size(axes[0])
    chunks = values.reshape((parts, values.shape[0] // parts) + values.shape[1:])
    mine = jnp.sum(lax.all_to_all(chunks, axes[0], 0, 0, tiled=False), axis=0)
    mine = scattered_sum_nested(mine, axes[1:], inner_axes)
    return lax.all_gather(mine, axes[0], tiled=True)


def halves_sum(values, axis):
    width = values.shape[1] // 2
    left = gathered_sum(values[:, :width], (axis,))
    right = gathered_sum(values[:, width:], (axis,))
    return jnp.concatenate([left, right], axis=1)


def column_block_pairs(rows, cols, shift):
    group = rows // cols
    pairs = []
    for r in range(rows):
        for c in range(cols):
            target_row = group * c + (r % group - shift) % group
            pairs.append((r * cols + c, target_row * cols + r // group))
    return pairs


def staged_route(rows, cols):
    sizes = (4, rows // 4, cols // 2, 2)
    if rows % 4 or cols % 2 or sizes[2] % sizes[0]:
        return None
    k = sizes[2] // sizes[0]

    def split(i):
        return (i // (sizes[1] * sizes[2] * 2), (i // (sizes[2] * 2)) % sizes[1], (i // 2) % sizes[2], i % 2)

    def join(x, z, y, core):
        return ((x * sizes[1] + z) * sizes[2] + y) * 2 + core

    def hop(i):
        x, z, y, core = split(i)
        return join(y // k, z, k * x + y % k, core)

    return [(i, hop(i)) for i in range(rows * cols)]


def to_column_blocks(values, rows, cols, all_axes, row_index):
    group = rows // cols
    first = staged_route(rows, cols)
    if first is None:
        rounds = [
            lax.ppermute(values, all_axes, column_block_pairs(rows, cols, shift))
            for shift in range(group)
        ]
    else:
        moved = lax.ppermute(values, all_axes, first)
        rounds = []
        for shift in range(group):
            final = dict(column_block_pairs(rows, cols, shift))
            rounds.append(lax.ppermute(moved, all_axes, [(mid, final[i]) for i, mid in first]))
    offset = row_index % group
    blocks = []
    for part in range(group):
        block = rounds[0]
        for shift in range(1, group):
            block = jnp.where((part - offset) % group == shift, rounds[shift], block)
        blocks.append(block)
    return jnp.concatenate(blocks, axis=values.ndim - 1)


def make_shards(row_axes, col_axes, rows, cols):
    all_axes = tuple(row_axes) + tuple(col_axes)

    def shards(matrix, reflectors, factors):
        current = matrix
        v_rows = reflectors[0]
        factor = factors[0]
        row_index = lax.axis_index(tuple(row_axes))
        v_cols = to_column_blocks(v_rows, rows, cols, all_axes, row_index)
        col_sums = scattered_sum_nested(contract(v_rows, current, 1, 0), row_axes[:0:-1], row_axes[:1])
        partial_value = contract(v_cols, current, 1, 1)
        partial_inner = contract(v_cols, col_sums, 1, 1)
        width = partial_value.shape[1]
        sums = split_sum(gathered_sum(jnp.concatenate([partial_value, partial_inner], axis=1), col_axes[1:]), col_axes[0], col_axes[1])
        row_sums = sums[:, :width]
        inner = sums[:, width:]
        x_rows = contract(factor, row_sums, 0, 0)
        x_cols = contract(factor, col_sums, 0, 0)
        projected = contract(inner, factor, 0, 0)
        mixing = contract(projected, factor, 0, 0)
        w_rows = x_rows - 0.5 * contract(mixing, v_rows, 1, 0)
        w_cols = x_cols - 0.5 * contract(mixing, v_cols, 1, 0)
        current = current - contract(v_rows, w_cols, 0, 0) - contract(w_rows, v_cols, 0, 0)
        return (current, jnp.stack([w_rows]))

    return shards


def solution(mesh):
    rows, cols = mesh.shape["row"], mesh.shape["col"]
    row_axes, col_axes = ("x", "za", "zb"), ("y", "core")
    fine = Mesh(mesh.devices.reshape((4, rows // 8, 2, cols // 2, 2)), row_axes + col_axes)
    return jax.shard_map(
        make_shards(row_axes, col_axes, rows, cols),
        mesh=fine,
        in_specs=(P(row_axes, col_axes), P(None, None, row_axes), P()),
        out_specs=(P(row_axes, col_axes), P(None, None, row_axes)),
        check_vma=False,
    )
```

```python
import jax
import jax.numpy as jnp
from jax import lax
from jax.sharding import Mesh
from jax.sharding import PartitionSpec as P


def contract(left_side, right_side, left_dim, right_dim):
    return lax.dot_general(
        left_side,
        right_side,
        (((left_dim,), (right_dim,)), ((), ())),
        precision=lax.Precision.HIGHEST,
        preferred_element_type=jnp.float32,
    )


def gathered_sum(values, axes):
    for axis in axes:
        values = jnp.sum(lax.all_gather(values, axis), axis=0)
    return values


def split_sum(values, axis, split_axis):
    width = values.shape[1] // 2
    mine = jnp.where(lax.axis_index(split_axis) == 0, values[:, :width], values[:, width:])
    total = gathered_sum(mine, (axis,))
    both = lax.all_gather(total, split_axis)
    return jnp.concatenate([both[0], both[1]], axis=1)


def scattered_sum(values, axis, parts):
    chunks = values.reshape((parts, values.shape[0] // parts) + values.shape[1:])
    mine = jnp.sum(lax.all_to_all(chunks, axis, 0, 0, tiled=False), axis=0)
    return lax.all_gather(mine, axis, tiled=True)


def scattered_sum_nested(values, axes, inner_axes=()):
    if not axes:
        return gathered_sum(values, inner_axes)
    parts = lax.axis_size(axes[0])
    chunks = values.reshape((parts, values.shape[0] // parts) + values.shape[1:])
    mine = jnp.sum(lax.all_to_all(chunks, axes[0], 0, 0, tiled=False), axis=0)
    mine = scattered_sum_nested(mine, axes[1:], inner_axes)
    return lax.all_gather(mine, axes[0], tiled=True)


def halves_sum(values, axis):
    width = values.shape[1] // 2
    left = gathered_sum(values[:, :width], (axis,))
    right = gathered_sum(values[:, width:], (axis,))
    return jnp.concatenate([left, right], axis=1)


def column_block_pairs(rows, cols, shift):
    group = rows // cols
    pairs = []
    for r in range(rows):
        for c in range(cols):
            target_row = group * c + (r % group - shift) % group
            pairs.append((r * cols + c, target_row * cols + r // group))
    return pairs


def staged_route(rows, cols):
    sizes = (4, rows // 4, cols // 2, 2)
    if rows % 4 or cols % 2 or sizes[2] % sizes[0]:
        return None
    k = sizes[2] // sizes[0]

    def split(i):
        return (i // (sizes[1] * sizes[2] * 2), (i // (sizes[2] * 2)) % sizes[1], (i // 2) % sizes[2], i % 2)

    def join(x, z, y, core):
        return ((x * sizes[1] + z) * sizes[2] + y) * 2 + core

    def hop(i):
        x, z, y, core = split(i)
        return join(y // k, z, k * x + y % k, core)

    return [(i, hop(i)) for i in range(rows * cols)]


def to_column_blocks(values, rows, cols, all_axes, row_index):
    group = rows // cols
    first = staged_route(rows, cols)
    if first is None:
        rounds = [
            lax.ppermute(values, all_axes, column_block_pairs(rows, cols, shift))
            for shift in range(group)
        ]
    else:
        moved = lax.ppermute(values, all_axes, first)
        rounds = []
        for shift in range(group):
            final = dict(column_block_pairs(rows, cols, shift))
            rounds.append(lax.ppermute(moved, all_axes, [(mid, final[i]) for i, mid in first]))
    offset = row_index % group
    blocks = []
    for part in range(group):
        block = rounds[0]
        for shift in range(1, group):
            block = jnp.where((part - offset) % group == shift, rounds[shift], block)
        blocks.append(block)
    return jnp.concatenate(blocks, axis=values.ndim - 1)


def make_shards(row_axes, col_axes, rows, cols):
    all_axes = tuple(row_axes) + tuple(col_axes)

    def shards(matrix, reflectors, factors):
        current = matrix
        v_rows = reflectors[0]
        factor = factors[0]
        row_index = lax.axis_index(tuple(row_axes))
        v_cols = to_column_blocks(v_rows, rows, cols, all_axes, row_index)
        col_sums = scattered_sum_nested(contract(v_rows, current, 1, 0), row_axes[:0:-1], row_axes[:1])
        partial_value = contract(v_cols, current, 1, 1)
        partial_inner = contract(v_cols, col_sums, 1, 1)
        width = partial_value.shape[1]
        sums = split_sum(gathered_sum(jnp.concatenate([partial_value, partial_inner], axis=1), col_axes[1:]), col_axes[0], col_axes[1])
        row_sums = sums[:, :width]
        inner = sums[:, width:]
        x_rows = contract(factor, row_sums, 0, 0)
        x_cols = contract(factor, col_sums, 0, 0)
        projected = contract(inner, factor, 0, 0)
        mixing = contract(projected, factor, 0, 0)
        w_rows = x_rows - 0.5 * contract(mixing, v_rows, 1, 0)
        w_cols = x_cols - 0.5 * contract(mixing, v_cols, 1, 0)
        current = current - contract(jnp.concatenate([v_rows, w_rows], axis=0), jnp.concatenate([w_cols, v_cols], axis=0), 0, 0)
        return (current, jnp.stack([w_rows]))

    return shards


def solution(mesh):
    rows, cols = mesh.shape["row"], mesh.shape["col"]
    row_axes, col_axes = ("x", "za", "zb"), ("y", "core")
    fine = Mesh(mesh.devices.reshape((4, rows // 8, 2, cols // 2, 2)), row_axes + col_axes)
    return jax.shard_map(
        make_shards(row_axes, col_axes, rows, cols),
        mesh=fine,
        in_specs=(P(row_axes, col_axes), P(None, None, row_axes), P()),
        out_specs=(P(row_axes, col_axes), P(None, None, row_axes)),
        check_vma=False,
    )
```

```python
import jax
import jax.numpy as jnp
from jax import lax
from jax.sharding import Mesh
from jax.sharding import PartitionSpec as P


def contract(left_side, right_side, left_dim, right_dim):
    return lax.dot_general(
        left_side,
        right_side,
        (((left_dim,), (right_dim,)), ((), ())),
        precision=lax.Precision.HIGHEST,
        preferred_element_type=jnp.float32,
    )


def gathered_sum(values, axes):
    for axis in axes:
        values = jnp.sum(lax.all_gather(values, axis), axis=0)
    return values


def split_sum(values, axis, split_axis):
    width = values.shape[1] // 2
    mine = jnp.where(lax.axis_index(split_axis) == 0, values[:, :width], values[:, width:])
    total = gathered_sum(mine, (axis,))
    both = lax.all_gather(total, split_axis)
    return jnp.concatenate([both[0], both[1]], axis=1)


def scattered_sum(values, axis, parts):
    chunks = values.reshape((parts, values.shape[0] // parts) + values.shape[1:])
    mine = jnp.sum(lax.all_to_all(chunks, axis, 0, 0, tiled=False), axis=0)
    return lax.all_gather(mine, axis, tiled=True)


def scattered_sum_nested(values, axes, inner_axes=()):
    if not axes:
        return gathered_sum(values, inner_axes)
    parts = lax.axis_size(axes[0])
    chunks = values.reshape((parts, values.shape[0] // parts) + values.shape[1:])
    mine = jnp.sum(lax.all_to_all(chunks, axes[0], 0, 0, tiled=False), axis=0)
    mine = scattered_sum_nested(mine, axes[1:], inner_axes)
    return lax.all_gather(mine, axes[0], tiled=True)


def halves_sum(values, axis):
    width = values.shape[1] // 2
    left = gathered_sum(values[:, :width], (axis,))
    right = gathered_sum(values[:, width:], (axis,))
    return jnp.concatenate([left, right], axis=1)


def column_block_pairs(rows, cols, shift):
    group = rows // cols
    pairs = []
    for r in range(rows):
        for c in range(cols):
            target_row = group * c + (r % group - shift) % group
            pairs.append((r * cols + c, target_row * cols + r // group))
    return pairs


def staged_route(rows, cols):
    sizes = (4, rows // 4, cols // 2, 2)
    if rows % 4 or cols % 2 or sizes[2] % sizes[0]:
        return None
    k = sizes[2] // sizes[0]

    def split(i):
        return (i // (sizes[1] * sizes[2] * 2), (i // (sizes[2] * 2)) % sizes[1], (i // 2) % sizes[2], i % 2)

    def join(x, z, y, core):
        return ((x * sizes[1] + z) * sizes[2] + y) * 2 + core

    def hop(i):
        x, z, y, core = split(i)
        return join(y // k, z, k * x + y % k, core)

    return [(i, hop(i)) for i in range(rows * cols)]


def to_column_blocks(values, rows, cols, all_axes, row_index):
    group = rows // cols
    first = staged_route(rows, cols)
    if first is None:
        rounds = [
            lax.ppermute(values, all_axes, column_block_pairs(rows, cols, shift))
            for shift in range(group)
        ]
    else:
        moved = lax.ppermute(values, all_axes, first)
        rounds = []
        for shift in range(group):
            final = dict(column_block_pairs(rows, cols, shift))
            rounds.append(lax.ppermute(moved, all_axes, [(mid, final[i]) for i, mid in first]))
    offset = row_index % group
    blocks = []
    for part in range(group):
        block = rounds[0]
        for shift in range(1, group):
            block = jnp.where((part - offset) % group == shift, rounds[shift], block)
        blocks.append(block)
    return jnp.concatenate(blocks, axis=values.ndim - 1)


def make_shards(row_axes, col_axes, rows, cols):
    all_axes = tuple(row_axes) + tuple(col_axes)

    def shards(matrix, reflectors, factors):
        current = matrix
        v_rows = reflectors[0]
        factor = factors[0]
        row_index = lax.axis_index(tuple(row_axes))
        chunks = contract(v_rows, current, 1, 0)
        first = row_axes[-1]
        parts = lax.axis_size(first)
        chunks = chunks.reshape((parts, chunks.shape[0] // parts) + chunks.shape[1:])
        mine = jnp.sum(lax.all_to_all(chunks, first, 0, 0, tiled=False), axis=0)
        mine, v_sent = lax.optimization_barrier((mine, v_rows))
        v_cols = to_column_blocks(v_sent, rows, cols, all_axes, row_index)
        mine = scattered_sum_nested(mine, row_axes[-2:0:-1], row_axes[:1])
        col_sums = lax.all_gather(mine, first, tiled=True)
        partial_value = contract(v_cols, current, 1, 1)
        partial_inner = contract(v_cols, col_sums, 1, 1)
        width = partial_value.shape[1]
        sums = split_sum(gathered_sum(jnp.concatenate([partial_value, partial_inner], axis=1), col_axes[1:]), col_axes[0], col_axes[1])
        row_sums = sums[:, :width]
        inner = sums[:, width:]
        x_rows = contract(factor, row_sums, 0, 0)
        x_cols = contract(factor, col_sums, 0, 0)
        projected = contract(inner, factor, 0, 0)
        mixing = contract(projected, factor, 0, 0)
        w_rows = x_rows - 0.5 * contract(mixing, v_rows, 1, 0)
        w_cols = x_cols - 0.5 * contract(mixing, v_cols, 1, 0)
        current = current - contract(jnp.concatenate([v_rows, w_rows], axis=0), jnp.concatenate([w_cols, v_cols], axis=0), 0, 0)
        return (current, jnp.stack([w_rows]))

    return shards


def solution(mesh):
    rows, cols = mesh.shape["row"], mesh.shape["col"]
    row_axes, col_axes = ("x", "za", "zb"), ("y", "core")
    fine = Mesh(mesh.devices.reshape((4, rows // 8, 2, cols // 2, 2)), row_axes + col_axes)
    return jax.shard_map(
        make_shards(row_axes, col_axes, rows, cols),
        mesh=fine,
        in_specs=(P(row_axes, col_axes), P(None, None, row_axes), P()),
        out_specs=(P(row_axes, col_axes), P(None, None, row_axes)),
        check_vma=False,
    )
```

```python
import jax
import jax.numpy as jnp
from jax import lax
from jax.sharding import Mesh
from jax.sharding import PartitionSpec as P


def contract(left_side, right_side, left_dim, right_dim):
    return lax.dot_general(
        left_side,
        right_side,
        (((left_dim,), (right_dim,)), ((), ())),
        precision=lax.Precision.HIGHEST,
        preferred_element_type=jnp.float32,
    )


def gathered_sum(values, axes):
    for axis in axes:
        values = jnp.sum(lax.all_gather(values, axis), axis=0)
    return values


def split_sum(values, axis, split_axis):
    width = values.shape[1] // 2
    mine = jnp.where(lax.axis_index(split_axis) == 0, values[:, :width], values[:, width:])
    total = gathered_sum(mine, (axis,))
    both = lax.all_gather(total, split_axis)
    return jnp.concatenate([both[0], both[1]], axis=1)


def scattered_sum(values, axis, parts):
    chunks = values.reshape((parts, values.shape[0] // parts) + values.shape[1:])
    mine = jnp.sum(lax.all_to_all(chunks, axis, 0, 0, tiled=False), axis=0)
    return lax.all_gather(mine, axis, tiled=True)


def scattered_sum_nested(values, axes, inner_axes=()):
    if not axes:
        return gathered_sum(values, inner_axes)
    parts = lax.axis_size(axes[0])
    chunks = values.reshape((parts, values.shape[0] // parts) + values.shape[1:])
    mine = jnp.sum(lax.all_to_all(chunks, axes[0], 0, 0, tiled=False), axis=0)
    mine = scattered_sum_nested(mine, axes[1:], inner_axes)
    return lax.all_gather(mine, axes[0], tiled=True)


def halves_sum(values, axis):
    width = values.shape[1] // 2
    left = gathered_sum(values[:, :width], (axis,))
    right = gathered_sum(values[:, width:], (axis,))
    return jnp.concatenate([left, right], axis=1)


def column_block_pairs(rows, cols, shift):
    group = rows // cols
    pairs = []
    for r in range(rows):
        for c in range(cols):
            target_row = group * c + (r % group - shift) % group
            pairs.append((r * cols + c, target_row * cols + r // group))
    return pairs


def staged_route(rows, cols):
    sizes = (4, rows // 4, cols // 2, 2)
    if rows % 4 or cols % 2 or sizes[2] % sizes[0]:
        return None
    k = sizes[2] // sizes[0]

    def split(i):
        return (i // (sizes[1] * sizes[2] * 2), (i // (sizes[2] * 2)) % sizes[1], (i // 2) % sizes[2], i % 2)

    def join(x, z, y, core):
        return ((x * sizes[1] + z) * sizes[2] + y) * 2 + core

    def hop(i):
        x, z, y, core = split(i)
        return join(y // k, z, k * x + y % k, core)

    return [(i, hop(i)) for i in range(rows * cols)]


def to_column_blocks(values, rows, cols, all_axes, row_index):
    group = rows // cols
    first = staged_route(rows, cols)
    if first is None:
        rounds = [
            lax.ppermute(values, all_axes, column_block_pairs(rows, cols, shift))
            for shift in range(group)
        ]
    else:
        moved = lax.ppermute(values, all_axes, first)
        rounds = []
        for shift in range(group):
            final = dict(column_block_pairs(rows, cols, shift))
            rounds.append(lax.ppermute(moved, all_axes, [(mid, final[i]) for i, mid in first]))
    offset = row_index % group
    blocks = []
    for part in range(group):
        block = rounds[0]
        for shift in range(1, group):
            block = jnp.where((part - offset) % group == shift, rounds[shift], block)
        blocks.append(block)
    return jnp.concatenate(blocks, axis=values.ndim - 1)


def second_hops(moved, rows, cols, all_axes, row_index):
    group = rows // cols
    first = staged_route(rows, cols)
    rounds = []
    for shift in range(group):
        final = dict(column_block_pairs(rows, cols, shift))
        rounds.append(lax.ppermute(moved, all_axes, [(mid, final[i]) for i, mid in first]))
    offset = row_index % group
    blocks = []
    for part in range(group):
        block = rounds[0]
        for shift in range(1, group):
            block = jnp.where((part - offset) % group == shift, rounds[shift], block)
        blocks.append(block)
    return jnp.concatenate(blocks, axis=moved.ndim - 1)


def make_shards(row_axes, col_axes, rows, cols):
    all_axes = tuple(row_axes) + tuple(col_axes)

    def shards(matrix, reflectors, factors):
        current = matrix
        v_rows = reflectors[0]
        factor = factors[0]
        row_index = lax.axis_index(tuple(row_axes))
        chunks = contract(v_rows, current, 1, 0)
        first = row_axes[-1]
        parts = lax.axis_size(first)
        chunks = chunks.reshape((parts, chunks.shape[0] // parts) + chunks.shape[1:])
        mine = jnp.sum(lax.all_to_all(chunks, first, 0, 0, tiled=False), axis=0)
        mine, v_sent = lax.optimization_barrier((mine, v_rows))
        moved = lax.ppermute(v_sent, all_axes, staged_route(rows, cols))
        second = row_axes[-2]
        parts2 = lax.axis_size(second)
        chunks = mine.reshape((parts2, mine.shape[0] // parts2) + mine.shape[1:])
        mine = jnp.sum(lax.all_to_all(chunks, second, 0, 0, tiled=False), axis=0)
        mine = gathered_sum(mine, row_axes[:1])
        mine, moved = lax.optimization_barrier((mine, moved))
        v_cols = second_hops(moved, rows, cols, all_axes, row_index)
        mine = lax.all_gather(mine, second, tiled=True)
        col_sums = lax.all_gather(mine, first, tiled=True)
        partial_value = contract(v_cols, current, 1, 1)
        partial_inner = contract(v_cols, col_sums, 1, 1)
        width = partial_value.shape[1]
        sums = split_sum(gathered_sum(jnp.concatenate([partial_value, partial_inner], axis=1), col_axes[1:]), col_axes[0], col_axes[1])
        row_sums = sums[:, :width]
        inner = sums[:, width:]
        x_rows = contract(factor, row_sums, 0, 0)
        x_cols = contract(factor, col_sums, 0, 0)
        projected = contract(inner, factor, 0, 0)
        mixing = contract(projected, factor, 0, 0)
        w_rows = x_rows - 0.5 * contract(mixing, v_rows, 1, 0)
        w_cols = x_cols - 0.5 * contract(mixing, v_cols, 1, 0)
        current = current - contract(jnp.concatenate([v_rows, w_rows], axis=0), jnp.concatenate([w_cols, v_cols], axis=0), 0, 0)
        return (current, jnp.stack([w_rows]))

    return shards


def solution(mesh):
    rows, cols = mesh.shape["row"], mesh.shape["col"]
    row_axes, col_axes = ("x", "za", "zb"), ("y", "core")
    fine = Mesh(mesh.devices.reshape((4, rows // 8, 2, cols // 2, 2)), row_axes + col_axes)
    return jax.shard_map(
        make_shards(row_axes, col_axes, rows, cols),
        mesh=fine,
        in_specs=(P(row_axes, col_axes), P(None, None, row_axes), P()),
        out_specs=(P(row_axes, col_axes), P(None, None, row_axes)),
        check_vma=False,
    )
```
